256 devices in a mesh: pair: 32 (over z, x_lo, core), grp: 8 (over y, x_hi).
Axes of the slice: x: 4 (x_hi: 2, x_lo: 2; x = x_hi * 2 + x_lo), y: 4, z: 8, core: 2. Of those that a mesh axis runs over, the one named last changes fastest.
Arguments:
- amplitudes: float32 [8, 224, 2048], P('grp', 'pair'), may hold values from -6 to 6
- integrals: float32 [2048, 65536], P('grp', 'pair'), may hold values from -0.375 to 0.375
- owner_blocks: int32 [16], replicated, may hold values from 0 to 15, each once
- occ_pairs: int32 [8, 2, 224], P('grp'), may hold values from 0 to 63, as said below
- vir_pairs: int32 [2, 65536], replicated, may hold values from 0 to 511, as said below
- occ_energy: float32 [64], replicated, may hold values from -1.5 to -0.5
- vir_energy: float32 [512], replicated, may hold values from 0.2 to 1.5
Outputs:
- ladder: float32 [8, 224, 65536], P('grp', 'pair')
The draws below stay inside these ranges and needn't reach their ends.
Inputs may be any that keep to these rules, and one draw needn't show every extreme that they name: `occ_pairs`: each column is a pair i<j; no pair occurs twice. `vir_pairs`: each column is a pair a<b; no pair occurs twice. `owner_blocks`: a permutation.
All inputs are finite; a program needn't handle non-finite values.
Results may differ from the reference program's by a relative error of at most 0.000071.
Values sent between devices are 32-bit elements; how exact they have to be, the bound alone decides.
No kernel may reach another device: no remote copies, remote signals or barrier semaphores. Data moves between devices by JAX's collectives and lax.ppermute only.
A program may use at most 64 MiB of HBM per device.

```python
import jax
import jax.numpy as jnp
import numpy as np
from jax import lax

NOCC = 64
NVIR = 512
CD = 2048
BLOCKS = 16
IJ_G = 224
IJ = 1792
AB = 65536
N_GRP = 8


def draw_occ_pairs(key, part):
    first, second = np.triu_indices(NOCC, 1)
    table = jnp.asarray(np.stack([first, second]), dtype=jnp.int32)
    picked = jax.random.permutation(key, table.shape[1])[:IJ]
    chosen = jnp.take(table, picked, axis=1)
    return jnp.transpose(chosen.reshape(2, -1, IJ_G), (1, 0, 2)).astype(jnp.int32)


def draw_vir_pairs(key, part):
    first, second = np.triu_indices(NVIR, 1)
    table = jnp.asarray(np.stack([first, second]), dtype=jnp.int32)
    picked = jax.random.permutation(jax.random.fold_in(key, 7), table.shape[1])[:AB]
    return jnp.take(table, picked, axis=1).astype(jnp.int32)


def block_levels(rng, extent, shards, smallest, top_value):
    gain = 1.0
    for dim, parts in shards:
        steps = jax.random.uniform(jax.random.fold_in(jax.random.fold_in(rng, 6), dim), (parts,), jnp.float32, smallest / len(shards), top_value / len(shards))
        gain = gain * jnp.repeat(jnp.exp(steps), extent[dim] // parts).reshape((-1,) + (1,) * (len(extent) - 1 - dim))
    return gain


def centred(own_key, extent, scale, most, cuts=(), kind=jnp.bfloat16):
    level = block_levels(own_key, extent, cuts, -0.22, 0.18) if cuts else 1.0
    result = jax.random.normal(own_key, extent, jnp.float32) * scale * level
    return jnp.minimum(jnp.maximum(result, -most), most).astype(kind)


def setup_inputs(seed: int = 0) -> dict:
    streams_of = jax.random.split(jax.random.key(seed), 8)
    return {
        "amplitudes": centred(streams_of[0], (N_GRP, IJ_G, CD), 1.0, 6.0, ((0, 8), (1, 32)), jnp.float32),
        "integrals": centred(streams_of[1], (CD, AB), (CD // 8) ** -0.5, 0.375, ((0, 8), (1, 32)), jnp.float32),
        "owner_blocks": jax.random.permutation(streams_of[2], BLOCKS).astype(jnp.int32),
        "occ_pairs": draw_occ_pairs(jax.random.fold_in(streams_of[7], 71), 0),
        "vir_pairs": draw_vir_pairs(jax.random.fold_in(streams_of[7], 71), 0),
        "occ_energy": jnp.clip(jax.random.uniform(streams_of[5], (NOCC,), jnp.float32, -1.5, -0.5), -1.5, -0.5),
        "vir_energy": jnp.clip(jax.random.uniform(streams_of[6], (NVIR,), jnp.float32, 0.2, 1.5), 0.2, 1.5),
    }


def reference(amplitudes, integrals, owner_blocks, occ_pairs, vir_pairs, occ_energy, vir_energy):
    groups = amplitudes.shape[0]
    width = amplitudes.shape[2]
    nblocks = owner_blocks.shape[0]
    tau = amplitudes.reshape(-1, nblocks, width // nblocks)
    permuted = jnp.take(tau, owner_blocks, axis=1).reshape(-1, width)
    work = jnp.dot(permuted, integrals, precision=lax.Precision.HIGHEST, preferred_element_type=jnp.float32)
    occ_flat = jnp.transpose(occ_pairs, (1, 0, 2)).reshape(2, -1)
    occ_sum = jnp.take(occ_energy, occ_flat[0]) + jnp.take(occ_energy, occ_flat[1])
    vir_sum = jnp.take(vir_energy, vir_pairs[0]) + jnp.take(vir_energy, vir_pairs[1])
    ladder = work / (occ_sum[:, None] - vir_sum[None, :])
    return ladder.reshape(groups, amplitudes.shape[1], -1)
```

```python
import jax
import jax.numpy as jnp
import numpy as np
from jax import lax
from jax.sharding import Mesh, PartitionSpec as P

N_CHUNK = 4


def pair_energies(energy, pairs):
    return jnp.take(energy, pairs[0]) + jnp.take(energy, pairs[1])


def on_device(amplitudes, integrals, owner_blocks, occ_pairs, vir_pairs, occ_energy, vir_energy):
    rows_l = amplitudes.shape[1]
    width = amplitudes.shape[2]
    block = integrals.shape[0]
    columns = integrals.shape[1]
    nblocks = owner_blocks.shape[0]
    sub = width // nblocks
    per_block = block // sub
    ny = lax.axis_size("gy")
    nx = lax.axis_size("gx")
    npair = lax.axis_size("pair")
    gx = lax.axis_index("gx")
    p = lax.axis_index("pair")

    def half_blocks(x):
        m = jnp.arange(ny * per_block, dtype=jnp.int32)
        b = ((m // per_block) * nx + x) * per_block + m % per_block
        return jnp.take(owner_blocks, b)

    tau = amplitudes[0].reshape(rows_l, nblocks, sub)

    def select(x):
        return jnp.take(tau, half_blocks(x), axis=1).reshape(rows_l, -1)

    mine = select(gx)
    other = select(1 - gx)
    swap = [(0, 1), (1, 0)]
    got = lax.ppermute(other, "gx", swap)
    both = jnp.where(gx == 0, jnp.stack([mine, got]), jnp.stack([got, mine]))
    spread = jnp.broadcast_to(both[None], (npair,) + both.shape)
    t_all = lax.all_to_all(spread, "pair", 0, 0, tiled=True)
    lhs = t_all.reshape(npair * nx * rows_l, -1)

    occ_sum = pair_energies(occ_energy, occ_pairs[0]).reshape(npair, rows_l)
    vir_local = lax.dynamic_slice_in_dim(vir_pairs, p * columns, columns, 1)
    vir_sum = pair_energies(vir_energy, vir_local)

    w = columns // N_CHUNK
    outs = []
    for c in range(N_CHUNK):
        piece = lax.all_gather(integrals[:, c * w:(c + 1) * w], "gy", axis=0, tiled=True)
        part = jnp.dot(lhs, piece, precision=lax.Precision.HIGHEST, preferred_element_type=jnp.float32)
        part = part.reshape(npair, nx, rows_l, w)
        keep = lax.dynamic_index_in_dim(part, gx, 1, keepdims=False)
        send = lax.dynamic_index_in_dim(part, 1 - gx, 1, keepdims=False)
        work = keep + lax.ppermute(send, "gx", swap)
        payload = work / (occ_sum[:, :, None] - vir_sum[None, None, c * w:(c + 1) * w])
        outs.append(lax.all_to_all(payload, "pair", 0, 0, tiled=True))
    res = jnp.stack(outs, axis=2)
    res = jnp.transpose(res, (1, 0, 2, 3)).reshape(1, rows_l, npair * columns)
    return res


def solution(mesh):
    devs = np.asarray(mesh.devices)
    npair, ngrp = devs.shape
    nx = 2
    sub_mesh = Mesh(devs.reshape(npair, ngrp // nx, nx), ("pair", "gy", "gx"))
    g = ("gy", "gx")
    return jax.shard_map(
        on_device,
        mesh=sub_mesh,
        in_specs=(
            P(g, "pair", None),
            P(g, "pair"),
            P(),
            P(g, None, None),
            P(),
            P(),
            P(),
        ),
        out_specs=P(g, "pair", None),
        check_vma=False,
    )
```

```python
import jax
import jax.numpy as jnp
import numpy as np
from jax import lax
from jax.sharding import Mesh, PartitionSpec as P

N_CHUNK = 4


def lookup(energy, idx):
    k = jnp.arange(energy.shape[0], dtype=idx.dtype)
    return jnp.sum(jnp.where(idx[..., None] == k, energy, 0.0), axis=-1)


def pair_energies(energy, pairs):
    return lookup(energy, pairs[0]) + lookup(energy, pairs[1])


def on_device(amplitudes, integrals, owner_blocks, occ_pairs, vir_pairs, occ_energy, vir_energy):
    rows_l = amplitudes.shape[1]
    width = amplitudes.shape[2]
    block = integrals.shape[0]
    columns = integrals.shape[1]
    nblocks = owner_blocks.shape[0]
    sub = width // nblocks
    per_block = block // sub
    ny = lax.axis_size("gy")
    nx = lax.axis_size("gx")
    npair = lax.axis_size("pair")
    gx = lax.axis_index("gx")
    p = lax.axis_index("pair")

    def half_blocks(x):
        m = jnp.arange(ny * per_block, dtype=jnp.int32)
        b = ((m // per_block) * nx + x) * per_block + m % per_block
        return jnp.take(owner_blocks, b)

    tau = amplitudes[0].reshape(rows_l, nblocks, sub)

    def select(x):
        return jnp.take(tau, half_blocks(x), axis=1).reshape(rows_l, -1)

    mine = select(gx)
    other = select(1 - gx)
    swap = [(0, 1), (1, 0)]
    got = lax.ppermute(other, "gx", swap)
    both = jnp.where(gx == 0, jnp.stack([mine, got]), jnp.stack([got, mine]))
    spread = jnp.broadcast_to(both[None], (npair,) + both.shape)
    t_all = lax.all_to_all(spread, "pair", 0, 0, tiled=True)
    lhs = t_all.reshape(npair * nx * rows_l, -1)

    occ_sum = pair_energies(occ_energy, occ_pairs[0]).reshape(npair, rows_l)
    vir_local = lax.dynamic_slice_in_dim(vir_pairs, p * columns, columns, 1)
    vir_sum = pair_energies(vir_energy, vir_local)

    w = columns // N_CHUNK
    outs = []
    works = []
    for c in range(N_CHUNK):
        piece = lax.all_gather(integrals[:, c * w:(c + 1) * w], "gy", axis=0, tiled=True)
        if c >= 1:
            piece, works[c - 1] = lax.optimization_barrier((piece, works[c - 1]))
        if c >= 2:
            piece, outs[c - 2] = lax.optimization_barrier((piece, outs[c - 2]))
        part = jnp.dot(lhs, piece, precision=lax.Precision.HIGHEST, preferred_element_type=jnp.float32)
        part = part.reshape(npair, nx, rows_l, w)
        keep = lax.dynamic_index_in_dim(part, gx, 1, keepdims=False)
        send = lax.dynamic_index_in_dim(part, 1 - gx, 1, keepdims=False)
        works.append(keep + lax.ppermute(send, "gx", swap))
        payload = works[c] / (occ_sum[:, :, None] - vir_sum[None, None, c * w:(c + 1) * w])
        outs.append(lax.all_to_all(payload, "pair", 0, 0, tiled=True))
    res = jnp.stack(outs, axis=2)
    res = jnp.transpose(res, (1, 0, 2, 3)).reshape(1, rows_l, npair * columns)
    return res


def solution(mesh):
    devs = np.asarray(mesh.devices)
    npair, ngrp = devs.shape
    nx = 2
    sub_mesh = Mesh(devs.reshape(npair, ngrp // nx, nx), ("pair", "gy", "gx"))
    g = ("gy", "gx")
    return jax.shard_map(
        on_device,
        mesh=sub_mesh,
        in_specs=(
            P(g, "pair", None),
            P(g, "pair"),
            P(),
            P(g, None, None),
            P(),
            P(),
            P(),
        ),
        out_specs=P(g, "pair", None),
        check_vma=False,
    )
```

```python
import jax
import jax.numpy as jnp
import numpy as np
from jax import lax
from jax.sharding import Mesh, PartitionSpec as P

N_CHUNK = 4


def lookup(energy, idx):
    k = jnp.arange(energy.shape[0], dtype=idx.dtype)
    return jnp.sum(jnp.where(idx[..., None] == k, energy, 0.0), axis=-1)


def pair_energies(energy, pairs):
    return lookup(energy, pairs[0]) + lookup(energy, pairs[1])


def ring_gather(x, n):
    assert n == 4
    right = [(i, (i + 1) % n) for i in range(n)]
    left = [(i, (i - 1) % n) for i in range(n)]
    h = x.shape[0] // 2
    from_left = lax.ppermute(x, "gy", right)
    from_right = lax.ppermute(x, "gy", left)
    far_a = lax.ppermute(from_left[:h], "gy", right)
    far_b = lax.ppermute(from_right[h:], "gy", left)
    return jnp.concatenate([x, from_right, far_a, far_b, from_left], axis=0)


def on_device(amplitudes, integrals, owner_blocks, occ_pairs, vir_pairs, occ_energy, vir_energy):
    rows_l = amplitudes.shape[1]
    width = amplitudes.shape[2]
    block = integrals.shape[0]
    columns = integrals.shape[1]
    nblocks = owner_blocks.shape[0]
    sub = width // nblocks
    per_block = block // sub
    ny = lax.axis_size("gy")
    nx = lax.axis_size("gx")
    npair = lax.axis_size("pair")
    gx = lax.axis_index("gx")
    p = lax.axis_index("pair")

    gy = lax.axis_index("gy")

    def half_blocks(x):
        m = jnp.arange(ny * per_block, dtype=jnp.int32)
        b = (((gy + m // per_block) % ny) * nx + x) * per_block + m % per_block
        return jnp.take(owner_blocks, b)

    tau = amplitudes[0].reshape(rows_l, nblocks, sub)

    def select(x):
        return jnp.take(tau, half_blocks(x), axis=1).reshape(rows_l, -1)

    mine = select(gx)
    other = select(1 - gx)
    swap = [(0, 1), (1, 0)]
    got = lax.ppermute(other, "gx", swap)
    both = jnp.where(gx == 0, jnp.stack([mine, got]), jnp.stack([got, mine]))
    spread = jnp.broadcast_to(both[None], (npair,) + both.shape)
    t_all = lax.all_to_all(spread, "pair", 0, 0, tiled=True)
    lhs = t_all.reshape(npair * nx * rows_l, -1)

    occ_sum = pair_energies(occ_energy, occ_pairs[0]).reshape(npair, rows_l)
    vir_local = lax.dynamic_slice_in_dim(vir_pairs, p * columns, columns, 1)
    vir_sum = pair_energies(vir_energy, vir_local)

    w = columns // N_CHUNK
    outs = []
    works = []
    for c in range(N_CHUNK):
        piece = ring_gather(integrals[:, c * w:(c + 1) * w], ny)
        if c >= 1:
            piece, works[c - 1] = lax.optimization_barrier((piece, works[c - 1]))
        if c >= 2:
            piece, outs[c - 2] = lax.optimization_barrier((piece, outs[c - 2]))
        part = jnp.dot(lhs, piece, precision=lax.Precision.HIGHEST, preferred_element_type=jnp.float32)
        part = part.reshape(npair, nx, rows_l, w)
        keep = lax.dynamic_index_in_dim(part, gx, 1, keepdims=False)
        send = lax.dynamic_index_in_dim(part, 1 - gx, 1, keepdims=False)
        works.append(keep + lax.ppermute(send, "gx", swap))
        payload = works[c] / (occ_sum[:, :, None] - vir_sum[None, None, c * w:(c + 1) * w])
        outs.append(lax.all_to_all(payload, "pair", 0, 0, tiled=True))
    res = jnp.stack(outs, axis=2)
    res = jnp.transpose(res, (1, 0, 2, 3)).reshape(1, rows_l, npair * columns)
    return res


def solution(mesh):
    devs = np.asarray(mesh.devices)
    npair, ngrp = devs.shape
    nx = 2
    sub_mesh = Mesh(devs.reshape(npair, ngrp // nx, nx), ("pair", "gy", "gx"))
    g = ("gy", "gx")
    return jax.shard_map(
        on_device,
        mesh=sub_mesh,
        in_specs=(
            P(g, "pair", None),
            P(g, "pair"),
            P(),
            P(g, None, None),
            P(),
            P(),
            P(),
        ),
        out_specs=P(g, "pair", None),
        check_vma=False,
    )
```

```python
import jax
import jax.numpy as jnp
import numpy as np
from jax import lax
from jax.sharding import Mesh, PartitionSpec as P

CHUNK_PARTS = (4, 5, 5, 2)


def lookup(energy, idx):
    k = jnp.arange(energy.shape[0], dtype=idx.dtype)
    return jnp.sum(jnp.where(idx[..., None] == k, energy, 0.0), axis=-1)


def pair_energies(energy, pairs):
    return lookup(energy, pairs[0]) + lookup(energy, pairs[1])


def on_device(amplitudes, integrals, owner_blocks, occ_pairs, vir_pairs, occ_energy, vir_energy):
    rows_l = amplitudes.shape[1]
    width = amplitudes.shape[2]
    block = integrals.shape[0]
    columns = integrals.shape[1]
    nblocks = owner_blocks.shape[0]
    sub = width // nblocks
    per_block = block // sub
    ny = lax.axis_size("gy")
    nx = lax.axis_size("gx")
    npair = lax.axis_size("pair")
    gx = lax.axis_index("gx")
    p = lax.axis_index("pair")

    def half_blocks(x):
        m = jnp.arange(ny * per_block, dtype=jnp.int32)
        b = ((m // per_block) * nx + x) * per_block + m % per_block
        return jnp.take(owner_blocks, b)

    tau = amplitudes[0].reshape(rows_l, nblocks, sub)

    def select(x):
        return jnp.take(tau, half_blocks(x), axis=1).reshape(rows_l, -1)

    mine = select(gx)
    other = select(1 - gx)
    swap = [(0, 1), (1, 0)]
    got = lax.ppermute(other, "gx", swap)
    both = jnp.where(gx == 0, jnp.stack([mine, got]), jnp.stack([got, mine]))
    spread = jnp.broadcast_to(both[None], (npair,) + both.shape)
    t_all = lax.all_to_all(spread, "pair", 0, 0, tiled=True)
    lhs = t_all.reshape(npair * nx * rows_l, -1)

    occ_sum = pair_energies(occ_energy, occ_pairs[0]).reshape(npair, rows_l)
    vir_local = lax.dynamic_slice_in_dim(vir_pairs, p * columns, columns, 1)
    vir_sum = pair_energies(vir_energy, vir_local)

    unit = columns // sum(CHUNK_PARTS)
    bounds = np.cumsum((0,) + CHUNK_PARTS) * unit
    outs = []
    works = []
    for c in range(len(CHUNK_PARTS)):
        lo, hi = int(bounds[c]), int(bounds[c + 1])
        w = hi - lo
        piece = lax.all_gather(integrals[:, lo:hi], "gy", axis=0, tiled=True)
        if c >= 2:
            piece, outs[c - 2] = lax.optimization_barrier((piece, outs[c - 2]))
        part = jnp.dot(lhs, piece, precision=lax.Precision.HIGHEST, preferred_element_type=jnp.float32)
        part = part.reshape(npair, nx, rows_l, w)
        keep = lax.dynamic_index_in_dim(part, gx, 1, keepdims=False)
        send = lax.dynamic_index_in_dim(part, 1 - gx, 1, keepdims=False)
        works.append(keep + lax.ppermute(send, "gx", swap))
        payload = works[c] / (occ_sum[:, :, None] - vir_sum[None, None, lo:hi])
        outs.append(lax.all_to_all(payload, "pair", 0, 0, tiled=True))
    res = jnp.concatenate(outs, axis=2)
    res = jnp.transpose(res, (1, 0, 2)).reshape(1, rows_l, npair * columns)
    return res


def solution(mesh):
    devs = np.asarray(mesh.devices)
    npair, ngrp = devs.shape
    nx = 2
    sub_mesh = Mesh(devs.reshape(npair, ngrp // nx, nx), ("pair", "gy", "gx"))
    g = ("gy", "gx")
    return jax.shard_map(
        on_device,
        mesh=sub_mesh,
        in_specs=(
            P(g, "pair", None),
            P(g, "pair"),
            P(),
            P(g, None, None),
            P(),
            P(),
            P(),
        ),
        out_specs=P(g, "pair", None),
        check_vma=False,
    )
```

```python
import jax
import jax.numpy as jnp
import numpy as np
from jax import lax
from jax.sharding import Mesh, PartitionSpec as P

N_CHUNK = 4


def lookup(energy, idx):
    k = jnp.arange(energy.shape[0], dtype=idx.dtype)
    return jnp.sum(jnp.where(idx[..., None] == k, energy, 0.0), axis=-1)


def pair_energies(energy, pairs):
    return lookup(energy, pairs[0]) + lookup(energy, pairs[1])


def on_device(amplitudes, integrals, owner_blocks, occ_pairs, vir_pairs, occ_energy, vir_energy):
    rows_l = amplitudes.shape[1]
    width = amplitudes.shape[2]
    block = integrals.shape[0]
    columns = integrals.shape[1]
    nblocks = owner_blocks.shape[0]
    sub = width // nblocks
    per_block = block // sub
    ny = lax.axis_size("gy")
    nx = lax.axis_size("gx")
    npair = lax.axis_size("pair")
    gx = lax.axis_index("gx")
    p = lax.axis_index("pair")

    def half_blocks(x):
        m = jnp.arange(ny * per_block, dtype=jnp.int32)
        b = ((m // per_block) * nx + x) * per_block + m % per_block
        return jnp.take(owner_blocks, b)

    tau = amplitudes[0].reshape(rows_l, nblocks, sub)

    def select(x):
        return jnp.take(tau, half_blocks(x), axis=1).reshape(rows_l, -1)

    mine = select(gx)
    other = select(1 - gx)
    swap = [(0, 1), (1, 0)]
    got = lax.ppermute(other, "gx", swap)
    both = jnp.where(gx == 0, jnp.stack([mine, got]), jnp.stack([got, mine]))
    spread = jnp.broadcast_to(both[None], (npair,) + both.shape)
    t_all = lax.all_to_all(spread, "pair", 0, 0, tiled=True)
    lhs = t_all.reshape(npair * nx * rows_l, -1)

    occ_sum = pair_energies(occ_energy, occ_pairs[0]).reshape(npair, rows_l)
    vir_local = lax.dynamic_slice_in_dim(vir_pairs, p * columns, columns, 1)
    vir_sum = pair_energies(vir_energy, vir_local)

    occ_got = lax.ppermute(occ_sum, "gx", swap)
    occ_both = jnp.where(gx == 0, jnp.stack([occ_sum, occ_got], 1), jnp.stack([occ_got, occ_sum], 1))

    w = columns // N_CHUNK
    outs = []
    for c in range(N_CHUNK):
        piece = lax.all_gather(integrals[:, c * w:(c + 1) * w], "gy", axis=0, tiled=True)
        if c >= 2:
            piece, outs[c - 2] = lax.optimization_barrier((piece, outs[c - 2]))
        part = jnp.dot(lhs, piece, precision=lax.Precision.HIGHEST, preferred_element_type=jnp.float32)
        part = part.reshape(npair, nx, rows_l, w)
        payload = part / (occ_both[:, :, :, None] - vir_sum[None, None, None, c * w:(c + 1) * w])
        payload = payload.reshape(npair * nx, rows_l, w)
        outs.append(lax.all_to_all(payload, ("pair", "gx"), 0, 0, tiled=True))
    outs = [o.reshape(npair, nx, rows_l, w) for o in outs]
    outs = [o[:, 0] + o[:, 1] for o in outs]
    res = jnp.stack(outs, axis=2)
    res = jnp.transpose(res, (1, 0, 2, 3)).reshape(1, rows_l, npair * columns)
    return res


def solution(mesh):
    devs = np.asarray(mesh.devices)
    npair, ngrp = devs.shape
    nx = 2
    sub_mesh = Mesh(devs.reshape(npair, ngrp // nx, nx), ("pair", "gy", "gx"))
    g = ("gy", "gx")
    return jax.shard_map(
        on_device,
        mesh=sub_mesh,
        in_specs=(
            P(g, "pair", None),
            P(g, "pair"),
            P(),
            P(g, None, None),
            P(),
            P(),
            P(),
        ),
        out_specs=P(g, "pair", None),
        check_vma=False,
    )
```

```python
import jax
import jax.numpy as jnp
import numpy as np
from jax import lax
from jax.sharding import Mesh, PartitionSpec as P

N_CHUNK = 4


def lookup(energy, idx):
    k = jnp.arange(energy.shape[0], dtype=idx.dtype)
    return jnp.sum(jnp.where(idx[..., None] == k, energy, 0.0), axis=-1)


def pair_energies(energy, pairs):
    return lookup(energy, pairs[0]) + lookup(energy, pairs[1])


def on_device(amplitudes, integrals, owner_blocks, occ_pairs, vir_pairs, occ_energy, vir_energy):
    rows_l = amplitudes.shape[1]
    width = amplitudes.shape[2]
    block = integrals.shape[0]
    columns = integrals.shape[1]
    nblocks = owner_blocks.shape[0]
    sub = width // nblocks
    per_block = block // sub
    ny = lax.axis_size("gy")
    nx = lax.axis_size("gx")
    npair = lax.axis_size("pair")
    gx = lax.axis_index("gx")
    p = lax.axis_index("pair")

    def half_blocks(x):
        m = jnp.arange(ny * per_block, dtype=jnp.int32)
        b = ((m // per_block) * nx + x) * per_block + m % per_block
        return jnp.take(owner_blocks, b)

    tau = amplitudes[0].reshape(rows_l, nblocks, sub)

    def select(x):
        return jnp.take(tau, half_blocks(x), axis=1).reshape(rows_l, -1)

    mine = select(gx)
    other = select(1 - gx)
    swap = [(0, 1), (1, 0)]
    got = lax.ppermute(other, "gx", swap)
    both = jnp.where(gx == 0, jnp.stack([mine, got]), jnp.stack([got, mine]))
    spread = jnp.broadcast_to(both[None], (npair,) + both.shape)
    t_all = lax.all_to_all(spread, "pair", 0, 0, tiled=True)
    lhs = t_all.reshape(npair * nx * rows_l, -1)

    occ_sum = pair_energies(occ_energy, occ_pairs[0]).reshape(npair, rows_l)
    vir_local = lax.dynamic_slice_in_dim(vir_pairs, p * columns, columns, 1)
    vir_sum = pair_energies(vir_energy, vir_local)

    w = columns // N_CHUNK
    outs = []
    works = []
    for c in range(N_CHUNK):
        piece = lax.all_gather(integrals[:, c * w:(c + 1) * w], "gy", axis=0, tiled=True)
        if c >= 1:
            piece, works[c - 1] = lax.optimization_barrier((piece, works[c - 1]))
        if c >= 2:
            piece, outs[c - 2] = lax.optimization_barrier((piece, outs[c - 2]))
        part = jnp.dot(lhs, piece, precision=lax.Precision.HIGH, preferred_element_type=jnp.float32)
        part = part.reshape(npair, nx, rows_l, w)
        keep = lax.dynamic_index_in_dim(part, gx, 1, keepdims=False)
        send = lax.dynamic_index_in_dim(part, 1 - gx, 1, keepdims=False)
        works.append(keep + lax.ppermute(send, "gx", swap))
        payload = works[c] / (occ_sum[:, :, None] - vir_sum[None, None, c * w:(c + 1) * w])
        outs.append(lax.all_to_all(payload, "pair", 0, 0, tiled=True))
    res = jnp.stack(outs, axis=2)
    res = jnp.transpose(res, (1, 0, 2, 3)).reshape(1, rows_l, npair * columns)
    return res


def solution(mesh):
    devs = np.asarray(mesh.devices)
    npair, ngrp = devs.shape
    nx = 2
    sub_mesh = Mesh(devs.reshape(npair, ngrp // nx, nx), ("pair", "gy", "gx"))
    g = ("gy", "gx")
    return jax.shard_map(
        on_device,
        mesh=sub_mesh,
        in_specs=(
            P(g, "pair", None),
            P(g, "pair"),
            P(),
            P(g, None, None),
            P(),
            P(),
            P(),
        ),
        out_specs=P(g, "pair", None),
        check_vma=False,
    )
```

```python
import jax
import jax.numpy as jnp
import numpy as np
from jax import lax
from jax.sharding import Mesh, PartitionSpec as P

CHUNK_PARTS = (6, 5, 5)


def lookup(energy, idx):
    k = jnp.arange(energy.shape[0], dtype=idx.dtype)
    return jnp.sum(jnp.where(idx[..., None] == k, energy, 0.0), axis=-1)


def pair_energies(energy, pairs):
    return lookup(energy, pairs[0]) + lookup(energy, pairs[1])


def on_device(amplitudes, integrals, owner_blocks, occ_pairs, vir_pairs, occ_energy, vir_energy):
    rows_l = amplitudes.shape[1]
    width = amplitudes.shape[2]
    block = integrals.shape[0]
    columns = integrals.shape[1]
    nblocks = owner_blocks.shape[0]
    sub = width // nblocks
    per_block = block // sub
    ny = lax.axis_size("gy")
    nx = lax.axis_size("gx")
    npair = lax.axis_size("pair")
    gx = lax.axis_index("gx")
    p = lax.axis_index("pair")

    def half_blocks(x):
        m = jnp.arange(ny * per_block, dtype=jnp.int32)
        b = ((m // per_block) * nx + x) * per_block + m % per_block
        return jnp.take(owner_blocks, b)

    tau = amplitudes[0].reshape(rows_l, nblocks, sub)

    def select(x):
        return jnp.take(tau, half_blocks(x), axis=1).reshape(rows_l, -1)

    mine = select(gx)
    other = select(1 - gx)
    swap = [(0, 1), (1, 0)]
    got = lax.ppermute(other, "gx", swap)
    both = jnp.where(gx == 0, jnp.stack([mine, got]), jnp.stack([got, mine]))
    spread = jnp.broadcast_to(both[None], (npair,) + both.shape)
    t_all = lax.all_to_all(spread, "pair", 0, 0, tiled=True)
    lhs = t_all.reshape(npair * nx * rows_l, -1)

    occ_sum = pair_energies(occ_energy, occ_pairs[0]).reshape(npair, rows_l)
    vir_local = lax.dynamic_slice_in_dim(vir_pairs, p * columns, columns, 1)
    vir_sum = pair_energies(vir_energy, vir_local)

    unit = columns // sum(CHUNK_PARTS)
    bounds = np.cumsum((0,) + CHUNK_PARTS) * unit
    outs = []
    works = []
    for c in range(len(CHUNK_PARTS)):
        lo, hi = int(bounds[c]), int(bounds[c + 1])
        w = hi - lo
        piece = lax.all_gather(integrals[:, lo:hi], "gy", axis=0, tiled=True)
        if c >= 1:
            piece, works[c - 1] = lax.optimization_barrier((piece, works[c - 1]))
        if c >= 2:
            piece, outs[c - 2] = lax.optimization_barrier((piece, outs[c - 2]))
        part = jnp.dot(lhs, piece, precision=lax.Precision.HIGH, preferred_element_type=jnp.float32)
        part = part.reshape(npair, nx, rows_l, w)
        keep = lax.dynamic_index_in_dim(part, gx, 1, keepdims=False)
        send = lax.dynamic_index_in_dim(part, 1 - gx, 1, keepdims=False)
        works.append(keep + lax.ppermute(send, "gx", swap))
        payload = works[c] / (occ_sum[:, :, None] - vir_sum[None, None, lo:hi])
        outs.append(lax.all_to_all(payload, "pair", 0, 0, tiled=True))
    res = jnp.concatenate(outs, axis=2)
    res = jnp.transpose(res, (1, 0, 2)).reshape(1, rows_l, npair * columns)
    return res


def solution(mesh):
    devs = np.asarray(mesh.devices)
    npair, ngrp = devs.shape
    nx = 2
    sub_mesh = Mesh(devs.reshape(npair, ngrp // nx, nx), ("pair", "gy", "gx"))
    g = ("gy", "gx")
    return jax.shard_map(
        on_device,
        mesh=sub_mesh,
        in_specs=(
            P(g, "pair", None),
            P(g, "pair"),
            P(),
            P(g, None, None),
            P(),
            P(),
            P(),
        ),
        out_specs=P(g, "pair", None),
        check_vma=False,
    )
```

```python
import jax
import jax.numpy as jnp
import numpy as np
from jax import lax
from jax.sharding import Mesh, PartitionSpec as P

CHUNK_PARTS = (6, 5, 5)


PAIR = ("pz", "pq")


def lookup(energy, idx):
    k = jnp.arange(energy.shape[0], dtype=idx.dtype)
    return jnp.sum(jnp.where(idx[..., None] == k, energy, 0.0), axis=-1)


def pair_energies(energy, pairs):
    return lookup(energy, pairs[0]) + lookup(energy, pairs[1])


def on_device(amplitudes, integrals, owner_blocks, occ_pairs, vir_pairs, occ_energy, vir_energy):
    rows_l = amplitudes.shape[1]
    width = amplitudes.shape[2]
    block = integrals.shape[0]
    columns = integrals.shape[1]
    nblocks = owner_blocks.shape[0]
    sub = width // nblocks
    per_block = block // sub
    ny = lax.axis_size("gy")
    nx = lax.axis_size("gx")
    nz = lax.axis_size("pz")
    nq = lax.axis_size("pq")
    npair = nz * nq
    gx = lax.axis_index("gx")
    p = lax.axis_index("pz") * nq + lax.axis_index("pq")

    def half_blocks(x):
        m = jnp.arange(ny * per_block, dtype=jnp.int32)
        b = ((m // per_block) * nx + x) * per_block + m % per_block
        return jnp.take(owner_blocks, b)

    tau = amplitudes[0].reshape(rows_l, nblocks, sub)

    def select(x):
        return jnp.take(tau, half_blocks(x), axis=1).reshape(rows_l, -1)

    mine = select(gx)
    other = select(1 - gx)
    swap = [(0, 1), (1, 0)]
    got = lax.ppermute(other, "gx", swap)
    both = jnp.where(gx == 0, jnp.stack([mine, got]), jnp.stack([got, mine]))
    near = lax.all_to_all(jnp.broadcast_to(both[None], (nq,) + both.shape), "pq", 0, 0, tiled=True)
    t_all = lax.all_to_all(jnp.broadcast_to(near[None], (nz,) + near.shape), "pz", 0, 0, tiled=True)
    lhs = t_all.reshape(npair * nx * rows_l, -1)

    occ_sum = pair_energies(occ_energy, occ_pairs[0]).reshape(npair, rows_l)
    vir_local = lax.dynamic_slice_in_dim(vir_pairs, p * columns, columns, 1)
    vir_sum = pair_energies(vir_energy, vir_local)

    unit = columns // sum(CHUNK_PARTS)
    bounds = np.cumsum((0,) + CHUNK_PARTS) * unit
    outs = []
    works = []
    for c in range(len(CHUNK_PARTS)):
        lo, hi = int(bounds[c]), int(bounds[c + 1])
        w = hi - lo
        piece = lax.all_gather(integrals[:, lo:hi], "gy", axis=0, tiled=True)
        if c >= 1:
            piece, works[c - 1] = lax.optimization_barrier((piece, works[c - 1]))
        if c >= 2:
            piece, outs[c - 2] = lax.optimization_barrier((piece, outs[c - 2]))
        part = jnp.dot(lhs, piece, precision=lax.Precision.HIGH, preferred_element_type=jnp.float32)
        part = part.reshape(npair, nx, rows_l, w)
        keep = lax.dynamic_index_in_dim(part, gx, 1, keepdims=False)
        send = lax.dynamic_index_in_dim(part, 1 - gx, 1, keepdims=False)
        works.append(keep + lax.ppermute(send, "gx", swap))
        payload = works[c] / (occ_sum[:, :, None] - vir_sum[None, None, lo:hi])
        outs.append(lax.all_to_all(payload, PAIR, 0, 0, tiled=True))
    res = jnp.concatenate(outs, axis=2)
    res = jnp.transpose(res, (1, 0, 2)).reshape(1, rows_l, npair * columns)
    return res


def solution(mesh):
    devs = np.asarray(mesh.devices)
    npair, ngrp = devs.shape
    nx = 2
    nq = 4
    sub_mesh = Mesh(devs.reshape(npair // nq, nq, ngrp // nx, nx), ("pz", "pq", "gy", "gx"))
    g = ("gy", "gx")
    return jax.shard_map(
        on_device,
        mesh=sub_mesh,
        in_specs=(
            P(g, PAIR, None),
            P(g, PAIR),
            P(),
            P(g, None, None),
            P(),
            P(),
            P(),
        ),
        out_specs=P(g, PAIR, None),
        check_vma=False,
    )
```

```python
import jax
import jax.numpy as jnp
import numpy as np
from jax import lax
from jax.sharding import Mesh, PartitionSpec as P

CHUNK_PARTS = (8, 4, 4)


def lookup(energy, idx):
    k = jnp.arange(energy.shape[0], dtype=idx.dtype)
    return jnp.sum(jnp.where(idx[..., None] == k, energy, 0.0), axis=-1)


def pair_energies(energy, pairs):
    return lookup(energy, pairs[0]) + lookup(energy, pairs[1])


def on_device(amplitudes, integrals, owner_blocks, occ_pairs, vir_pairs, occ_energy, vir_energy):
    rows_l = amplitudes.shape[1]
    width = amplitudes.shape[2]
    block = integrals.shape[0]
    columns = integrals.shape[1]
    nblocks = owner_blocks.shape[0]
    sub = width // nblocks
    per_block = block // sub
    ny = lax.axis_size("gy")
    nx = lax.axis_size("gx")
    npair = lax.axis_size("pair")
    gx = lax.axis_index("gx")
    p = lax.axis_index("pair")

    def half_blocks(x):
        m = jnp.arange(ny * per_block, dtype=jnp.int32)
        b = ((m // per_block) * nx + x) * per_block + m % per_block
        return jnp.take(owner_blocks, b)

    tau = amplitudes[0].reshape(rows_l, nblocks, sub)

    def select(x):
        return jnp.take(tau, half_blocks(x), axis=1).reshape(rows_l, -1)

    mine = select(gx)
    other = select(1 - gx)
    swap = [(0, 1), (1, 0)]
    got = lax.ppermute(other, "gx", swap)
    both = jnp.where(gx == 0, jnp.stack([mine, got]), jnp.stack([got, mine]))
    spread = jnp.broadcast_to(both[None], (npair,) + both.shape)
    t_all = lax.all_to_all(spread, "pair", 0, 0, tiled=True)
    lhs = t_all.reshape(npair * nx * rows_l, -1)

    occ_sum = pair_energies(occ_energy, occ_pairs[0]).reshape(npair, rows_l)
    vir_local = lax.dynamic_slice_in_dim(vir_pairs, p * columns, columns, 1)
    vir_sum = pair_energies(vir_energy, vir_local)

    unit = columns // sum(CHUNK_PARTS)
    bounds = np.cumsum((0,) + CHUNK_PARTS) * unit
    outs = []
    works = []
    for c in range(len(CHUNK_PARTS)):
        lo, hi = int(bounds[c]), int(bounds[c + 1])
        w = hi - lo
        piece = lax.all_gather(integrals[:, lo:hi], "gy", axis=0, tiled=True)
        if c >= 1:
            piece, works[c - 1] = lax.optimization_barrier((piece, works[c - 1]))
        if c >= 2:
            piece, outs[c - 2] = lax.optimization_barrier((piece, outs[c - 2]))
        part = jnp.dot(lhs, piece, precision=lax.Precision.HIGH, preferred_element_type=jnp.float32)
        part = part.reshape(npair, nx, rows_l, w)
        keep = lax.dynamic_index_in_dim(part, gx, 1, keepdims=False)
        send = lax.dynamic_index_in_dim(part, 1 - gx, 1, keepdims=False)
        works.append(keep + lax.ppermute(send, "gx", swap))
        payload = works[c] / (occ_sum[:, :, None] - vir_sum[None, None, lo:hi])
        outs.append(lax.all_to_all(payload, "pair", 0, 0, tiled=True))
    res = jnp.concatenate(outs, axis=2)
    res = jnp.transpose(res, (1, 0, 2)).reshape(1, rows_l, npair * columns)
    return res


def solution(mesh):
    devs = np.asarray(mesh.devices)
    npair, ngrp = devs.shape
    nx = 2
    sub_mesh = Mesh(devs.reshape(npair, ngrp // nx, nx), ("pair", "gy", "gx"))
    g = ("gy", "gx")
    return jax.shard_map(
        on_device,
        mesh=sub_mesh,
        in_specs=(
            P(g, "pair", None),
            P(g, "pair"),
            P(),
            P(g, None, None),
            P(),
            P(),
            P(),
        ),
        out_specs=P(g, "pair", None),
        check_vma=False,
    )
```

```python
import jax
import jax.numpy as jnp
import numpy as np
from jax import lax
from jax.sharding import Mesh, PartitionSpec as P

CHUNK_PARTS = (9, 4, 3)


def lookup(energy, idx):
    k = jnp.arange(energy.shape[0], dtype=idx.dtype)
    return jnp.sum(jnp.where(idx[..., None] == k, energy, 0.0), axis=-1)


def pair_energies(energy, pairs):
    return lookup(energy, pairs[0]) + lookup(energy, pairs[1])


def on_device(amplitudes, integrals, owner_blocks, occ_pairs, vir_pairs, occ_energy, vir_energy):
    rows_l = amplitudes.shape[1]
    width = amplitudes.shape[2]
    block = integrals.shape[0]
    columns = integrals.shape[1]
    nblocks = owner_blocks.shape[0]
    sub = width // nblocks
    per_block = block // sub
    ny = lax.axis_size("gy")
    nx = lax.axis_size("gx")
    npair = lax.axis_size("pair")
    gx = lax.axis_index("gx")
    p = lax.axis_index("pair")

    def half_blocks(x):
        m = jnp.arange(ny * per_block, dtype=jnp.int32)
        b = ((m // per_block) * nx + x) * per_block + m % per_block
        return jnp.take(owner_blocks, b)

    tau = amplitudes[0].reshape(rows_l, nblocks, sub)

    def select(x):
        return jnp.take(tau, half_blocks(x), axis=1).reshape(rows_l, -1)

    mine = select(gx)
    other = select(1 - gx)
    swap = [(0, 1), (1, 0)]
    got = lax.ppermute(other, "gx", swap)
    both = jnp.where(gx == 0, jnp.stack([mine, got]), jnp.stack([got, mine]))
    spread = jnp.broadcast_to(both[None], (npair,) + both.shape)
    t_all = lax.all_to_all(spread, "pair", 0, 0, tiled=True)
    lhs = t_all.reshape(npair * nx * rows_l, -1)

    occ_sum = pair_energies(occ_energy, occ_pairs[0]).reshape(npair, rows_l)
    vir_local = lax.dynamic_slice_in_dim(vir_pairs, p * columns, columns, 1)
    vir_sum = pair_energies(vir_energy, vir_local)

    unit = columns // sum(CHUNK_PARTS)
    bounds = np.cumsum((0,) + CHUNK_PARTS) * unit
    outs = []
    works = []
    for c in range(len(CHUNK_PARTS)):
        lo, hi = int(bounds[c]), int(bounds[c + 1])
        w = hi - lo
        piece = lax.all_gather(integrals[:, lo:hi], "gy", axis=0, tiled=True)
        if c >= 1:
            piece, works[c - 1] = lax.optimization_barrier((piece, works[c - 1]))
        if c >= 2:
            piece, outs[c - 2] = lax.optimization_barrier((piece, outs[c - 2]))
        part = jnp.dot(lhs, piece, precision=lax.Precision.HIGH, preferred_element_type=jnp.float32)
        part = part.reshape(npair, nx, rows_l, w)
        keep = lax.dynamic_index_in_dim(part, gx, 1, keepdims=False)
        send = lax.dynamic_index_in_dim(part, 1 - gx, 1, keepdims=False)
        works.append(keep + lax.ppermute(send, "gx", swap))
        payload = works[c] / (occ_sum[:, :, None] - vir_sum[None, None, lo:hi])
        outs.append(lax.all_to_all(payload, "pair", 0, 0, tiled=True))
    res = jnp.concatenate(outs, axis=2)
    res = jnp.transpose(res, (1, 0, 2)).reshape(1, rows_l, npair * columns)
    return res


def solution(mesh):
    devs = np.asarray(mesh.devices)
    npair, ngrp = devs.shape
    nx = 2
    sub_mesh = Mesh(devs.reshape(npair, ngrp // nx, nx), ("pair", "gy", "gx"))
    g = ("gy", "gx")
    return jax.shard_map(
        on_device,
        mesh=sub_mesh,
        in_specs=(
            P(g, "pair", None),
            P(g, "pair"),
            P(),
            P(g, None, None),
            P(),
            P(),
            P(),
        ),
        out_specs=P(g, "pair", None),
        check_vma=False,
    )
```

```python
import jax
import jax.numpy as jnp
import numpy as np
from jax import lax
from jax.sharding import Mesh, PartitionSpec as P

CHUNK_PARTS = (10, 3, 3)


def lookup(energy, idx):
    k = jnp.arange(energy.shape[0], dtype=idx.dtype)
    return jnp.sum(jnp.where(idx[..., None] == k, energy, 0.0), axis=-1)


def pair_energies(energy, pairs):
    return lookup(energy, pairs[0]) + lookup(energy, pairs[1])


def on_device(amplitudes, integrals, owner_blocks, occ_pairs, vir_pairs, occ_energy, vir_energy):
    rows_l = amplitudes.shape[1]
    width = amplitudes.shape[2]
    block = integrals.shape[0]
    columns = integrals.shape[1]
    nblocks = owner_blocks.shape[0]
    sub = width // nblocks
    per_block = block // sub
    ny = lax.axis_size("gy")
    nx = lax.axis_size("gx")
    npair = lax.axis_size("pair")
    gx = lax.axis_index("gx")
    p = lax.axis_index("pair")

    def half_blocks(x):
        m = jnp.arange(ny * per_block, dtype=jnp.int32)
        b = ((m // per_block) * nx + x) * per_block + m % per_block
        return jnp.take(owner_blocks, b)

    tau = amplitudes[0].reshape(rows_l, nblocks, sub)

    def select(x):
        return jnp.take(tau, half_blocks(x), axis=1).reshape(rows_l, -1)

    mine = select(gx)
    other = select(1 - gx)
    swap = [(0, 1), (1, 0)]
    got = lax.ppermute(other, "gx", swap)
    both = jnp.where(gx == 0, jnp.stack([mine, got]), jnp.stack([got, mine]))
    spread = jnp.broadcast_to(both[None], (npair,) + both.shape)
    t_all = lax.all_to_all(spread, "pair", 0, 0, tiled=True)
    lhs = t_all.reshape(npair * nx * rows_l, -1)

    occ_sum = pair_energies(occ_energy, occ_pairs[0]).reshape(npair, rows_l)
    vir_local = lax.dynamic_slice_in_dim(vir_pairs, p * columns, columns, 1)
    vir_sum = pair_energies(vir_energy, vir_local)

    unit = columns // sum(CHUNK_PARTS)
    bounds = np.cumsum((0,) + CHUNK_PARTS) * unit
    outs = []
    works = []
    for c in range(len(CHUNK_PARTS)):
        lo, hi = int(bounds[c]), int(bounds[c + 1])
        w = hi - lo
        piece = lax.all_gather(integrals[:, lo:hi], "gy", axis=0, tiled=True)
        if c >= 1:
            piece, works[c - 1] = lax.optimization_barrier((piece, works[c - 1]))
        if c >= 2:
            piece, outs[c - 2] = lax.optimization_barrier((piece, outs[c - 2]))
        part = jnp.dot(lhs, piece, precision=lax.Precision.HIGH, preferred_element_type=jnp.float32)
        part = part.reshape(npair, nx, rows_l, w)
        keep = lax.dynamic_index_in_dim(part, gx, 1, keepdims=False)
        send = lax.dynamic_index_in_dim(part, 1 - gx, 1, keepdims=False)
        works.append(keep + lax.ppermute(send, "gx", swap))
        payload = works[c] / (occ_sum[:, :, None] - vir_sum[None, None, lo:hi])
        outs.append(lax.all_to_all(payload, "pair", 0, 0, tiled=True))
    res = jnp.concatenate(outs, axis=2)
    res = jnp.transpose(res, (1, 0, 2)).reshape(1, rows_l, npair * columns)
    return res


def solution(mesh):
    devs = np.asarray(mesh.devices)
    npair, ngrp = devs.shape
    nx = 2
    sub_mesh = Mesh(devs.reshape(npair, ngrp // nx, nx), ("pair", "gy", "gx"))
    g = ("gy", "gx")
    return jax.shard_map(
        on_device,
        mesh=sub_mesh,
        in_specs=(
            P(g, "pair", None),
            P(g, "pair"),
            P(),
            P(g, None, None),
            P(),
            P(),
            P(),
        ),
        out_specs=P(g, "pair", None),
        check_vma=False,
    )
```

```python
import jax
import jax.numpy as jnp
import numpy as np
from jax import lax
from jax.sharding import Mesh, PartitionSpec as P

CHUNK_PARTS = (9, 5, 2)


def lookup(energy, idx):
    k = jnp.arange(energy.shape[0], dtype=idx.dtype)
    return jnp.sum(jnp.where(idx[..., None] == k, energy, 0.0), axis=-1)


def pair_energies(energy, pairs):
    return lookup(energy, pairs[0]) + lookup(energy, pairs[1])


def on_device(amplitudes, integrals, owner_blocks, occ_pairs, vir_pairs, occ_energy, vir_energy):
    rows_l = amplitudes.shape[1]
    width = amplitudes.shape[2]
    block = integrals.shape[0]
    columns = integrals.shape[1]
    nblocks = owner_blocks.shape[0]
    sub = width // nblocks
    per_block = block // sub
    ny = lax.axis_size("gy")
    nx = lax.axis_size("gx")
    npair = lax.axis_size("pair")
    gx = lax.axis_index("gx")
    p = lax.axis_index("pair")

    def half_blocks(x):
        m = jnp.arange(ny * per_block, dtype=jnp.int32)
        b = ((m // per_block) * nx + x) * per_block + m % per_block
        return jnp.take(owner_blocks, b)

    tau = amplitudes[0].reshape(rows_l, nblocks, sub)

    def select(x):
        return jnp.take(tau, half_blocks(x), axis=1).reshape(rows_l, -1)

    mine = select(gx)
    other = select(1 - gx)
    swap = [(0, 1), (1, 0)]
    got = lax.ppermute(other, "gx", swap)
    both = jnp.where(gx == 0, jnp.stack([mine, got]), jnp.stack([got, mine]))
    spread = jnp.broadcast_to(both[None], (npair,) + both.shape)
    t_all = lax.all_to_all(spread, "pair", 0, 0, tiled=True)
    lhs = t_all.reshape(npair * nx * rows_l, -1)

    occ_sum = pair_energies(occ_energy, occ_pairs[0]).reshape(npair, rows_l)
    vir_local = lax.dynamic_slice_in_dim(vir_pairs, p * columns, columns, 1)
    vir_sum = pair_energies(vir_energy, vir_local)

    unit = columns // sum(CHUNK_PARTS)
    bounds = np.cumsum((0,) + CHUNK_PARTS) * unit
    outs = []
    works = []
    for c in range(len(CHUNK_PARTS)):
        lo, hi = int(bounds[c]), int(bounds[c + 1])
        w = hi - lo
        piece = lax.all_gather(integrals[:, lo:hi], "gy", axis=0, tiled=True)
        if c >= 1:
            piece, works[c - 1] = lax.optimization_barrier((piece, works[c - 1]))
        if c >= 2:
            piece, outs[c - 2] = lax.optimization_barrier((piece, outs[c - 2]))
        part = jnp.dot(lhs, piece, precision=lax.Precision.HIGH, preferred_element_type=jnp.float32)
        part = part.reshape(npair, nx, rows_l, w)
        keep = lax.dynamic_index_in_dim(part, gx, 1, keepdims=False)
        send = lax.dynamic_index_in_dim(part, 1 - gx, 1, keepdims=False)
        works.append(keep + lax.ppermute(send, "gx", swap))
        payload = works[c] / (occ_sum[:, :, None] - vir_sum[None, None, lo:hi])
        outs.append(lax.all_to_all(payload, "pair", 0, 0, tiled=True))
    res = jnp.concatenate(outs, axis=2)
    res = jnp.transpose(res, (1, 0, 2)).reshape(1, rows_l, npair * columns)
    return res


def solution(mesh):
    devs = np.asarray(mesh.devices)
    npair, ngrp = devs.shape
    nx = 2
    sub_mesh = Mesh(devs.reshape(npair, ngrp // nx, nx), ("pair", "gy", "gx"))
    g = ("gy", "gx")
    return jax.shard_map(
        on_device,
        mesh=sub_mesh,
        in_specs=(
            P(g, "pair", None),
            P(g, "pair"),
            P(),
            P(g, None, None),
            P(),
            P(),
            P(),
        ),
        out_specs=P(g, "pair", None),
        check_vma=False,
    )
```

```python
import jax
import jax.numpy as jnp
import numpy as np
from jax import lax
from jax.sharding import Mesh, PartitionSpec as P

CHUNK_PARTS = (9, 4, 3)


def lookup(energy, idx):
    k = jnp.arange(energy.shape[0], dtype=idx.dtype)
    return jnp.sum(jnp.where(idx[..., None] == k, energy, 0.0), axis=-1)


def pair_energies(energy, pairs):
    return lookup(energy, pairs[0]) + lookup(energy, pairs[1])


def on_device(amplitudes, integrals, owner_blocks, occ_pairs, vir_pairs, occ_energy, vir_energy):
    rows_l = amplitudes.shape[1]
    width = amplitudes.shape[2]
    block = integrals.shape[0]
    columns = integrals.shape[1]
    nblocks = owner_blocks.shape[0]
    sub = width // nblocks
    per_block = block // sub
    ny = lax.axis_size("gy")
    nx = lax.axis_size("gx")
    npair = lax.axis_size("pair")
    gx = lax.axis_index("gx")
    p = lax.axis_index("pair")

    def half_blocks(x):
        m = jnp.arange(ny * per_block, dtype=jnp.int32)
        b = ((m // per_block) * nx + x) * per_block + m % per_block
        return jnp.take(owner_blocks, b)

    tau = amplitudes[0].reshape(rows_l, nblocks, sub)

    def select(x):
        return jnp.take(tau, half_blocks(x), axis=1).reshape(rows_l, -1)

    halves = jnp.stack([select(x) for x in range(nx)])
    spread = jnp.broadcast_to(halves[None], (npair,) + halves.shape).reshape((npair * nx,) + halves.shape[1:])
    t_all = lax.all_to_all(spread, ("pair", "gx"), 0, 0, tiled=True)
    swap = [(0, 1), (1, 0)]
    lhs = t_all.reshape(npair * nx * rows_l, -1)

    occ_sum = pair_energies(occ_energy, occ_pairs[0]).reshape(npair, rows_l)
    vir_local = lax.dynamic_slice_in_dim(vir_pairs, p * columns, columns, 1)
    vir_sum = pair_energies(vir_energy, vir_local)

    unit = columns // sum(CHUNK_PARTS)
    bounds = np.cumsum((0,) + CHUNK_PARTS) * unit
    outs = []
    works = []
    for c in range(len(CHUNK_PARTS)):
        lo, hi = int(bounds[c]), int(bounds[c + 1])
        w = hi - lo
        piece = lax.all_gather(integrals[:, lo:hi], "gy", axis=0, tiled=True)
        if c >= 1:
            piece, works[c - 1] = lax.optimization_barrier((piece, works[c - 1]))
        if c >= 2:
            piece, outs[c - 2] = lax.optimization_barrier((piece, outs[c - 2]))
        part = jnp.dot(lhs, piece, precision=lax.Precision.HIGH, preferred_element_type=jnp.float32)
        part = part.reshape(npair, nx, rows_l, w)
        keep = lax.dynamic_index_in_dim(part, gx, 1, keepdims=False)
        send = lax.dynamic_index_in_dim(part, 1 - gx, 1, keepdims=False)
        works.append(keep + lax.ppermute(send, "gx", swap))
        payload = works[c] / (occ_sum[:, :, None] - vir_sum[None, None, lo:hi])
        outs.append(lax.all_to_all(payload, "pair", 0, 0, tiled=True))
    res = jnp.concatenate(outs, axis=2)
    res = jnp.transpose(res, (1, 0, 2)).reshape(1, rows_l, npair * columns)
    return res


def solution(mesh):
    devs = np.asarray(mesh.devices)
    npair, ngrp = devs.shape
    nx = 2
    sub_mesh = Mesh(devs.reshape(npair, ngrp // nx, nx), ("pair", "gy", "gx"))
    g = ("gy", "gx")
    return jax.shard_map(
        on_device,
        mesh=sub_mesh,
        in_specs=(
            P(g, "pair", None),
            P(g, "pair"),
            P(),
            P(g, None, None),
            P(),
            P(),
            P(),
        ),
        out_specs=P(g, "pair", None),
        check_vma=False,
    )
```

```python
import jax
import jax.numpy as jnp
import numpy as np
from jax import lax
from jax.sharding import Mesh, PartitionSpec as P

CHUNK_PARTS = (9, 4, 3)


def lookup(energy, idx):
    k = jnp.arange(energy.shape[0], dtype=idx.dtype)
    return jnp.sum(jnp.where(idx[..., None] == k, energy, 0.0), axis=-1)


def pair_energies(energy, pairs):
    return lookup(energy, pairs[0]) + lookup(energy, pairs[1])


def on_device(amplitudes, integrals, owner_blocks, occ_pairs, vir_pairs, occ_energy, vir_energy):
    rows_l = amplitudes.shape[1]
    width = amplitudes.shape[2]
    block = integrals.shape[0]
    columns = integrals.shape[1]
    nblocks = owner_blocks.shape[0]
    sub = width // nblocks
    per_block = block // sub
    ny = lax.axis_size("gy")
    nx = lax.axis_size("gx")
    npair = lax.axis_size("pair")
    gx = lax.axis_index("gx")
    p = lax.axis_index("pair")

    def half_blocks(x):
        m = jnp.arange(ny * per_block, dtype=jnp.int32)
        b = ((m // per_block) * nx + x) * per_block + m % per_block
        return jnp.take(owner_blocks, b)

    tau = amplitudes[0].reshape(rows_l, nblocks, sub)

    def select(x):
        return jnp.take(tau, half_blocks(x), axis=1).reshape(rows_l, -1)

    mine = select(gx)
    other = select(1 - gx)
    swap = [(0, 1), (1, 0)]
    got = lax.ppermute(other, "gx", swap)
    both = jnp.where(gx == 0, jnp.stack([mine, got]), jnp.stack([got, mine]))
    spread = jnp.broadcast_to(both[None], (npair,) + both.shape)
    t_all = lax.all_to_all(spread, "pair", 0, 0, tiled=True)
    lhs = t_all.reshape(npair * nx * rows_l, -1)

    occ_sum = pair_energies(occ_energy, occ_pairs[0]).reshape(npair, rows_l)
    vir_local = lax.dynamic_slice_in_dim(vir_pairs, p * columns, columns, 1)
    vir_sum = pair_energies(vir_energy, vir_local)

    unit = columns // sum(CHUNK_PARTS)
    bounds = np.cumsum((0,) + CHUNK_PARTS) * unit
    outs = []
    works = []
    for c in range(len(CHUNK_PARTS)):
        lo, hi = int(bounds[c]), int(bounds[c + 1])
        w = hi - lo
        piece = lax.all_gather(integrals[:, lo:hi], "gy", axis=0, tiled=True)
        if c >= 2:
            piece, works[c - 1] = lax.optimization_barrier((piece, works[c - 1]))
        if c >= 2:
            piece, outs[c - 2] = lax.optimization_barrier((piece, outs[c - 2]))
        part = jnp.dot(lhs, piece, precision=lax.Precision.HIGH, preferred_element_type=jnp.float32)
        part = part.reshape(npair, nx, rows_l, w)
        keep = lax.dynamic_index_in_dim(part, gx, 1, keepdims=False)
        send = lax.dynamic_index_in_dim(part, 1 - gx, 1, keepdims=False)
        works.append(keep + lax.ppermute(send, "gx", swap))
        payload = works[c] / (occ_sum[:, :, None] - vir_sum[None, None, lo:hi])
        outs.append(lax.all_to_all(payload, "pair", 0, 0, tiled=True))
    res = jnp.concatenate(outs, axis=2)
    res = jnp.transpose(res, (1, 0, 2)).reshape(1, rows_l, npair * columns)
    return res


def solution(mesh):
    devs = np.asarray(mesh.devices)
    npair, ngrp = devs.shape
    nx = 2
    sub_mesh = Mesh(devs.reshape(npair, ngrp // nx, nx), ("pair", "gy", "gx"))
    g = ("gy", "gx")
    return jax.shard_map(
        on_device,
        mesh=sub_mesh,
        in_specs=(
            P(g, "pair", None),
            P(g, "pair"),
            P(),
            P(g, None, None),
            P(),
            P(),
            P(),
        ),
        out_specs=P(g, "pair", None),
        check_vma=False,
    )
```
